256 devices in a mesh: prow: 64 (over x, z, core), pcol: 4 (over y).
Axes of the slice: x: 4, y: 4, z: 8, core: 2. Of those that a mesh axis runs over, the one named last changes fastest.
Arguments:
- right_side: float32 [512, 65536], P('pcol', 'prow'), may hold values from -6 to 6
- factor: float32 [65536, 2048], P('prow', 'pcol'), may hold values from -0.125 to 0.125
- inverses: float32 [2048, 512], replicated, as said below
Outputs:
- solved: float32 [512, 65536], P('pcol', 'prow')
The draws below stay inside these ranges and needn't reach their ends.
Inputs may be any that keep to these rules, and one draw needn't show every extreme that they name: Each 512 x 512 block of inverses is lower triangular with a positive diagonal.
All inputs are finite; a program needn't handle non-finite values.
Results may differ from the reference program's by a relative error of at most 0.0001.
Values sent between devices are 32-bit elements; how exact they have to be, the bound alone decides.
No kernel may reach another device: no remote copies, remote signals or barrier semaphores. Data moves between devices by JAX's collectives and lax.ppermute only.
A program may use at most 64 MiB of HBM per device.

```python
import jax
import jax.numpy as jnp
from jax import lax

NB = 512
STEPS = 4
NRHS = 512
RB_DEV = 2
M = 65536
N_PROW = 64


def draw_inverses(key, part):
    first_key, second_key = jax.random.split(jax.random.fold_in(key, 7))
    shape = (STEPS * NB, NB)
    offdiag = jax.random.normal(first_key, shape, jnp.float32) * (0.6 / NB ** 0.5)
    diagonal = jnp.exp(jax.random.uniform(second_key, (STEPS * NB, 1), jnp.float32, -0.6931472, 0.6931472))
    row_index = jnp.arange(STEPS * NB)[:, None] % NB
    col_index = jnp.arange(NB)[None, :]
    return jnp.where(row_index > col_index, offdiag, jnp.where(row_index == col_index, diagonal, 0.0)).astype(jnp.float32)


def shard_levels(rng, extent, cuts, smallest, largest):
    gain, own = 1.0, jax.random.fold_in(rng, 6)
    for dim, parts in cuts:
        heights = jnp.exp(jax.random.uniform(jax.random.fold_in(own, dim), (parts,), jnp.float32, smallest / len(cuts), largest / len(cuts)))
        gain = gain * jnp.repeat(heights, extent[dim] // parts).reshape([-1 if axis == dim else 1 for axis in range(len(extent))])
    return gain


def gaussian(key, shape, spread, most, cuts=(), dtype=jnp.bfloat16):
    loudness = shard_levels(key, shape, cuts, -0.22, 0.18) if cuts else 1.0
    values = jax.random.normal(key, shape, jnp.float32) * spread * loudness
    return jnp.minimum(jnp.maximum(values, -most), most).astype(dtype)


def setup_inputs(seed: int = 0) -> dict:
    key_list = jax.random.split(jax.random.key(seed), 4)
    return {
        "right_side": gaussian(key_list[0], (NRHS, M), 1.0, 6.0, ((0, 4), (1, 64)), jnp.float32),
        "factor": gaussian(key_list[1], (M, STEPS * NB), (STEPS * NB) ** -0.5, 0.125, ((0, 64), (1, 4)), jnp.float32),
        "inverses": draw_inverses(jax.random.fold_in(key_list[3], 71), 0),
    }


def contract(left, right):
    return lax.dot_general(left, right, (((1,), (1,)), ((), ())), precision=lax.Precision.HIGHEST, preferred_element_type=jnp.float32)


def reference(right_side, factor, inverses):
    total = NB * RB_DEV * N_PROW
    rhs_matrix = right_side.reshape(NRHS, N_PROW, RB_DEV, NB).transpose(0, 2, 1, 3).reshape(NRHS, total)
    lower = factor.reshape(N_PROW, RB_DEV, NB, STEPS * NB).transpose(1, 0, 2, 3).reshape(total, STEPS * NB)
    solved_list = []
    for section in range(STEPS):
        current = rhs_matrix[:, section * NB:(section + 1) * NB]
        for column in range(section):
            current = current - contract(solved_list[column], lower[section * NB:(section + 1) * NB, column * NB:(column + 1) * NB])
        solved_list.append(contract(current, inverses[section * NB:(section + 1) * NB]))
    trailing = rhs_matrix
    for column in range(STEPS):
        trailing = trailing - contract(solved_list[column], lower[:, column * NB:(column + 1) * NB])
    result = jnp.concatenate(solved_list + [trailing[:, STEPS * NB:]], axis=1)
    return result.reshape(NRHS, RB_DEV, N_PROW, NB).transpose(0, 2, 1, 3).reshape(NRHS, total)
```

```python
import jax
import jax.numpy as jnp
from jax import lax
from jax.sharding import PartitionSpec as P


def contract(left, right):
    return lax.dot_general(
        left,
        right,
        (((1,), (1,)), ((), ())),
        precision=lax.Precision.HIGHEST,
        preferred_element_type=jnp.float32,
    )


AXES = ("prow", "pcol")


def per_device(right_side, factor, inverses):
    block = factor.shape[1]
    rhs_width = right_side.shape[0]
    n_col = lax.axis_size("pcol")
    n_row = lax.axis_size("prow")
    steps = n_col
    row_at = lax.axis_index("prow")
    col_at = lax.axis_index("pcol")

    def at(p, c):
        return p * n_col + c

    top_rhs = right_side[:, :block]
    top_block = factor[:block]

    fetched = [top_block]
    for shift in range(1, n_col):
        pairs = [
            (at(i, j), at(i, (j + shift) % n_col))
            for i in range(1, steps)
            for j in range(i)
        ]
        fetched.append(lax.ppermute(top_block, AXES, pairs))
    fetched = jnp.stack(fetched)

    acc = jnp.zeros((rhs_width, block), jnp.float32)
    own = jnp.zeros((rhs_width, block), jnp.float32)
    for k in range(steps):
        solved = contract(top_rhs - acc, inverses[k * block : (k + 1) * block])
        own = jnp.where(row_at == k, solved, own)
        if k == steps - 1:
            break
        arrived = jnp.zeros_like(solved)
        for i in range(k + 1, steps):
            pairs = [(at(k, c), at(i, c)) for c in range(n_col)]
            arrived = arrived + lax.ppermute(solved, AXES, pairs)
        lower = lax.dynamic_index_in_dim(fetched, (col_at - k) % n_col, 0, keepdims=False)
        acc = acc + contract(arrived, lower)

    pairs = [(at(j, c), at(c, j)) for j in range(steps) for c in range(n_col) if j != c]
    piece = lax.ppermute(own, AXES, pairs)
    piece = jnp.where(row_at == col_at, own, piece)

    span = n_row // 2
    while span >= steps:
        pairs = [(p, p + span) for p in range(n_row) if p % (2 * span) < steps]
        arrived = lax.ppermute(piece, "prow", pairs)
        rel = row_at % (2 * span)
        piece = jnp.where((rel >= span) & (rel < span + steps), arrived, piece)
        span //= 2
    b0 = row_at % 2
    b1 = (row_at // 2) % 2
    other = lax.ppermute(piece, "prow", [(p, p ^ 2) for p in range(n_row)])
    pair = jnp.where(b1 == 0, jnp.concatenate([piece, other]), jnp.concatenate([other, piece]))
    theirs = lax.ppermute(pair, "prow", [(p, p ^ 1) for p in range(n_row)])
    mine_first = jnp.concatenate([pair[:rhs_width], theirs[:rhs_width], pair[rhs_width:], theirs[rhs_width:]])
    theirs_first = jnp.concatenate([theirs[:rhs_width], pair[:rhs_width], theirs[rhs_width:], pair[rhs_width:]])
    panel = jnp.where(b0 == 0, mine_first, theirs_first)

    updated = right_side - lax.psum_scatter(
        contract(panel, factor), "pcol", scatter_dimension=0, tiled=True
    )
    head_block = jnp.where(row_at < steps, own, updated[:, :block])
    return jnp.concatenate([head_block, updated[:, block:]], axis=1)


def solution(mesh):
    return jax.shard_map(
        per_device,
        mesh=mesh,
        in_specs=(P("pcol", "prow"), P("prow", "pcol"), P()),
        out_specs=P("pcol", "prow"),
        check_vma=False,
    )
```

```python
import jax
import jax.numpy as jnp
from jax import lax
from jax.sharding import PartitionSpec as P


def contract(left, right):
    return lax.dot_general(
        left,
        right,
        (((1,), (1,)), ((), ())),
        precision=lax.Precision.HIGHEST,
        preferred_element_type=jnp.float32,
    )


AXES = ("prow", "pcol")


def per_device(right_side, factor, inverses):
    block = factor.shape[1]
    rhs_width = right_side.shape[0]
    n_col = lax.axis_size("pcol")
    n_row = lax.axis_size("prow")
    steps = n_col
    row_at = lax.axis_index("prow")
    col_at = lax.axis_index("pcol")

    def at(p, c):
        return p * n_col + c

    top_rhs = right_side[:, :block]
    top_block = factor[:block]

    fetched = [top_block]
    for shift in range(1, n_col):
        pairs = [
            (at(i, j), at(i, (j + shift) % n_col))
            for i in range(1, steps)
            for j in range(i)
        ]
        fetched.append(lax.ppermute(top_block, AXES, pairs))
    fetched = jnp.stack(fetched)

    b0 = row_at % 2
    b1 = (row_at // 2) % 2
    acc = jnp.zeros((rhs_width, block), jnp.float32)
    own = jnp.zeros((rhs_width, block), jnp.float32)
    panels = []
    for k in range(steps):
        solved = contract(top_rhs - acc, inverses[k * block : (k + 1) * block])
        own = jnp.where(row_at == k, solved, own)
        if k < steps - 1:
            arrived = jnp.zeros_like(solved)
            for i in range(k + 1, steps):
                pairs = [(at(k, c), at(i, c)) for c in range(n_col)]
                arrived = arrived + lax.ppermute(solved, AXES, pairs)
            lower = lax.dynamic_index_in_dim(fetched, (col_at - k) % n_col, 0, keepdims=False)
            acc = acc + contract(arrived, lower)

        pairs = [(at(k, c), at(c, k)) for c in range(n_col) if c != k]
        piece = lax.ppermute(solved, AXES, pairs)
        piece = jnp.where(row_at == k, solved, piece)
        span = n_row // 2
        while span >= steps:
            pairs = [(at(p, k), at(p + span, k)) for p in range(n_row) if p % (2 * span) < steps]
            arrived = lax.ppermute(piece, AXES, pairs)
            rel = row_at % (2 * span)
            piece = jnp.where((rel >= span) & (rel < span + steps), arrived, piece)
            span //= 2
        other = lax.ppermute(piece, AXES, [(at(p, k), at(p ^ 2, k)) for p in range(n_row)])
        pair = jnp.where(b1 == 0, jnp.concatenate([piece, other]), jnp.concatenate([other, piece]))
        theirs = lax.ppermute(pair, AXES, [(at(p, k), at(p ^ 1, k)) for p in range(n_row)])
        mine_first = jnp.concatenate([pair[:rhs_width], theirs[:rhs_width], pair[rhs_width:], theirs[rhs_width:]])
        theirs_first = jnp.concatenate([theirs[:rhs_width], pair[:rhs_width], theirs[rhs_width:], pair[rhs_width:]])
        panels.append(jnp.where(b0 == 0, mine_first, theirs_first))

    panel = panels[0]
    for k in range(1, steps):
        panel = jnp.where(col_at == k, panels[k], panel)

    partial = contract(panel, factor)
    total = lax.dynamic_slice_in_dim(partial, col_at * rhs_width, rhs_width, 0)
    for shift in range(1, n_col):
        chunk = lax.dynamic_slice_in_dim(partial, ((col_at + shift) % n_col) * rhs_width, rhs_width, 0)
        total = total + lax.ppermute(chunk, "pcol", [(c, (c + shift) % n_col) for c in range(n_col)])
    updated = right_side - total
    head_block = jnp.where(row_at < steps, own, updated[:, :block])
    return jnp.concatenate([head_block, updated[:, block:]], axis=1)


def solution(mesh):
    return jax.shard_map(
        per_device,
        mesh=mesh,
        in_specs=(P("pcol", "prow"), P("prow", "pcol"), P()),
        out_specs=P("pcol", "prow"),
        check_vma=False,
    )
```

```python
import jax
import jax.numpy as jnp
from jax import lax
from jax.sharding import PartitionSpec as P


def contract(left, right):
    return lax.dot_general(
        left,
        right,
        (((1,), (1,)), ((), ())),
        precision=lax.Precision.HIGHEST,
        preferred_element_type=jnp.float32,
    )


AXES = ("prow", "pcol")


def per_device(right_side, factor, inverses):
    block = factor.shape[1]
    rhs_width = right_side.shape[0]
    n_col = lax.axis_size("pcol")
    n_row = lax.axis_size("prow")
    steps = n_col
    row_at = lax.axis_index("prow")
    col_at = lax.axis_index("pcol")

    def at(p, c):
        return p * n_col + c

    top_rhs = right_side[:, :block]
    top_block = factor[:block]

    fetched = [top_block]
    for shift in range(1, n_col):
        pairs = [
            (at(i, j), at(i, (j + shift) % n_col))
            for i in range(2, steps)
            for j in range(1, i)
        ]
        fetched.append(lax.ppermute(top_block, AXES, pairs))
    fetched = jnp.stack(fetched)

    solved = contract(top_rhs, inverses[:block])
    own = jnp.where(row_at == 0, solved, jnp.zeros_like(solved))
    pairs = [(at(0, c), at(c, 0)) for c in range(1, n_col)]
    piece = lax.ppermute(solved, AXES, pairs)
    piece = jnp.where(row_at == 0, solved, piece)
    b0 = row_at % 2
    b1 = (row_at // 2) % 2
    other = lax.ppermute(piece, AXES, [(at(p, 0), at(p ^ 2, 0)) for p in range(steps)])
    pair = jnp.where(b1 == 0, jnp.concatenate([piece, other]), jnp.concatenate([other, piece]))
    theirs = lax.ppermute(pair, AXES, [(at(p, 0), at(p ^ 1, 0)) for p in range(steps)])
    mine_first = jnp.concatenate([pair[:rhs_width], theirs[:rhs_width], pair[rhs_width:], theirs[rhs_width:]])
    theirs_first = jnp.concatenate([theirs[:rhs_width], pair[:rhs_width], theirs[rhs_width:], pair[rhs_width:]])
    first_panel = jnp.where(b0 == 0, mine_first, theirs_first)
    product = contract(first_panel, top_block)
    acc = jnp.where(col_at == 0, product[:rhs_width], jnp.zeros_like(solved))
    for shift in range(1, n_col):
        chunk = product[shift * rhs_width : (shift + 1) * rhs_width]
        pairs = [(at(i, 0), at(i, shift)) for i in range(1, steps)]
        acc = acc + lax.ppermute(chunk, AXES, pairs)

    for k in range(1, steps):
        solved = contract(top_rhs - acc, inverses[k * block : (k + 1) * block])
        own = jnp.where(row_at == k, solved, own)
        if k == steps - 1:
            break
        arrived = jnp.zeros_like(solved)
        for i in range(k + 1, steps):
            pairs = [(at(k, c), at(i, c)) for c in range(n_col)]
            arrived = arrived + lax.ppermute(solved, AXES, pairs)
        lower = lax.dynamic_index_in_dim(fetched, (col_at - k) % n_col, 0, keepdims=False)
        acc = acc + contract(arrived, lower)

    pairs = [(at(j, c), at(c, j)) for j in range(steps) for c in range(n_col) if j != c]
    piece = lax.ppermute(own, AXES, pairs)
    piece = jnp.where(row_at == col_at, own, piece)

    span = n_row // 2
    while span >= steps:
        pairs = [(p, p + span) for p in range(n_row) if p % (2 * span) < steps]
        arrived = lax.ppermute(piece, "prow", pairs)
        rel = row_at % (2 * span)
        piece = jnp.where((rel >= span) & (rel < span + steps), arrived, piece)
        span //= 2
    b0 = row_at % 2
    b1 = (row_at // 2) % 2
    other = lax.ppermute(piece, "prow", [(p, p ^ 2) for p in range(n_row)])
    pair = jnp.where(b1 == 0, jnp.concatenate([piece, other]), jnp.concatenate([other, piece]))
    theirs = lax.ppermute(pair, "prow", [(p, p ^ 1) for p in range(n_row)])
    mine_first = jnp.concatenate([pair[:rhs_width], theirs[:rhs_width], pair[rhs_width:], theirs[rhs_width:]])
    theirs_first = jnp.concatenate([theirs[:rhs_width], pair[:rhs_width], theirs[rhs_width:], pair[rhs_width:]])
    panel = jnp.where(b0 == 0, mine_first, theirs_first)

    updated = right_side - lax.psum_scatter(
        contract(panel, factor), "pcol", scatter_dimension=0, tiled=True
    )
    head_block = jnp.where(row_at < steps, own, updated[:, :block])
    return jnp.concatenate([head_block, updated[:, block:]], axis=1)


def solution(mesh):
    return jax.shard_map(
        per_device,
        mesh=mesh,
        in_specs=(P("pcol", "prow"), P("prow", "pcol"), P()),
        out_specs=P("pcol", "prow"),
        check_vma=False,
    )
```

```python
import jax
import jax.numpy as jnp
from jax import lax
from jax.sharding import PartitionSpec as P


def contract(left, right):
    return lax.dot_general(
        left,
        right,
        (((1,), (1,)), ((), ())),
        precision=lax.Precision.HIGHEST,
        preferred_element_type=jnp.float32,
    )


AXES = ("prow", "pcol")


def per_device(right_side, factor, inverses):
    block = factor.shape[1]
    rhs_width = right_side.shape[0]
    n_col = lax.axis_size("pcol")
    n_row = lax.axis_size("prow")
    steps = n_col
    row_at = lax.axis_index("prow")
    col_at = lax.axis_index("pcol")

    def at(p, c):
        return p * n_col + c

    top_rhs = right_side[:, :block]
    top_block = factor[:block]

    fetched = [top_block]
    for shift in range(1, n_col):
        pairs = [
            (at(i, j), at(i, (j + shift) % n_col))
            for i in range(1, steps)
            for j in range(i)
        ]
        fetched.append(lax.ppermute(top_block, AXES, pairs))
    fetched = jnp.stack(fetched)

    acc = jnp.zeros((rhs_width, block), jnp.float32)
    own = jnp.zeros((rhs_width, block), jnp.float32)
    for k in range(steps):
        solved = contract(top_rhs - acc, inverses[k * block : (k + 1) * block])
        own = jnp.where(row_at == k, solved, own)
        if k == steps - 1:
            break
        arrived = jnp.zeros_like(solved)
        for i in range(k + 1, steps):
            pairs = [(at(k, c), at(i, c)) for c in range(n_col)]
            arrived = arrived + lax.ppermute(solved, AXES, pairs)
        lower = lax.dynamic_index_in_dim(fetched, (col_at - k) % n_col, 0, keepdims=False)
        acc = acc + contract(arrived, lower)

    lower_all = lax.all_gather(factor, "pcol", axis=1, tiled=True)

    piece = own
    span = n_row // 2
    while span >= steps:
        pairs = [(p, p + span) for p in range(n_row) if p % (2 * span) < steps]
        arrived = lax.ppermute(piece, "prow", pairs)
        rel = row_at % (2 * span)
        piece = jnp.where((rel >= span) & (rel < span + steps), arrived, piece)
        span //= 2
    b0 = row_at % 2
    b1 = (row_at // 2) % 2
    other = lax.ppermute(piece, "prow", [(p, p ^ 2) for p in range(n_row)])
    pair = jnp.where(b1 == 0, jnp.concatenate([piece, other], axis=1), jnp.concatenate([other, piece], axis=1))
    theirs = lax.ppermute(pair, "prow", [(p, p ^ 1) for p in range(n_row)])
    mine, yours = (pair[:, :block], pair[:, block:]), (theirs[:, :block], theirs[:, block:])
    mine_first = jnp.concatenate([mine[0], yours[0], mine[1], yours[1]], axis=1)
    theirs_first = jnp.concatenate([yours[0], mine[0], yours[1], mine[1]], axis=1)
    panel = jnp.where(b0 == 0, mine_first, theirs_first)

    updated = right_side - contract(panel, lower_all)
    head_block = jnp.where(row_at < steps, own, updated[:, :block])
    return jnp.concatenate([head_block, updated[:, block:]], axis=1)


def solution(mesh):
    return jax.shard_map(
        per_device,
        mesh=mesh,
        in_specs=(P("pcol", "prow"), P("prow", "pcol"), P()),
        out_specs=P("pcol", "prow"),
        check_vma=False,
    )
```

```python
import jax
import jax.numpy as jnp
from jax import lax
from jax.sharding import PartitionSpec as P


def contract(left, right):
    return lax.dot_general(
        left,
        right,
        (((1,), (1,)), ((), ())),
        precision=lax.Precision.HIGHEST,
        preferred_element_type=jnp.float32,
    )


AXES = ("prow", "pcol")


def per_device(right_side, factor, inverses):
    block = factor.shape[1]
    rhs_width = right_side.shape[0]
    n_col = lax.axis_size("pcol")
    n_row = lax.axis_size("prow")
    steps = n_col
    row_at = lax.axis_index("prow")
    col_at = lax.axis_index("pcol")

    def at(p, c):
        return p * n_col + c

    top_rhs = right_side[:, :block]
    top_block = factor[:block]

    fetched = [top_block]
    for shift in range(1, n_col):
        pairs = [
            (at(i, j), at(i, (j + shift) % n_col))
            for i in range(1, steps)
            for j in range(i)
        ]
        fetched.append(lax.ppermute(top_block, AXES, pairs))
    fetched = jnp.stack(fetched)

    acc = jnp.zeros((rhs_width, block), jnp.float32)
    own = jnp.zeros((rhs_width, block), jnp.float32)
    for k in range(steps):
        solved = contract(top_rhs - acc, inverses[k * block : (k + 1) * block])
        own = jnp.where(row_at == k, solved, own)
        if k == steps - 1:
            break
        arrived = jnp.zeros_like(solved)
        for i in range(k + 1, steps):
            pairs = [(at(k, c), at(i, c)) for c in range(n_col)]
            arrived = arrived + lax.ppermute(solved, AXES, pairs)
        lower = lax.dynamic_index_in_dim(fetched, (col_at - k) % n_col, 0, keepdims=False)
        acc = acc + contract(arrived, lower)

    factor_later, _ = lax.optimization_barrier((factor, fetched))
    lower_all = lax.all_gather(factor_later, "pcol", axis=1, tiled=True)

    piece = own
    span = n_row // 2
    while span >= steps:
        pairs = [(p, p + span) for p in range(n_row) if p % (2 * span) < steps]
        arrived = lax.ppermute(piece, "prow", pairs)
        rel = row_at % (2 * span)
        piece = jnp.where((rel >= span) & (rel < span + steps), arrived, piece)
        span //= 2
    b0 = row_at % 2
    b1 = (row_at // 2) % 2
    other = lax.ppermute(piece, "prow", [(p, p ^ 2) for p in range(n_row)])
    pair = jnp.where(b1 == 0, jnp.concatenate([piece, other], axis=1), jnp.concatenate([other, piece], axis=1))
    theirs = lax.ppermute(pair, "prow", [(p, p ^ 1) for p in range(n_row)])
    mine, yours = (pair[:, :block], pair[:, block:]), (theirs[:, :block], theirs[:, block:])
    mine_first = jnp.concatenate([mine[0], yours[0], mine[1], yours[1]], axis=1)
    theirs_first = jnp.concatenate([yours[0], mine[0], yours[1], mine[1]], axis=1)
    panel = jnp.where(b0 == 0, mine_first, theirs_first)

    updated = right_side - contract(panel, lower_all)
    head_block = jnp.where(row_at < steps, own, updated[:, :block])
    return jnp.concatenate([head_block, updated[:, block:]], axis=1)


def solution(mesh):
    return jax.shard_map(
        per_device,
        mesh=mesh,
        in_specs=(P("pcol", "prow"), P("prow", "pcol"), P()),
        out_specs=P("pcol", "prow"),
        check_vma=False,
    )
```

```python
import jax
import jax.numpy as jnp
from jax import lax
from jax.sharding import PartitionSpec as P


def contract(left, right, precision=lax.Precision.HIGHEST):
    return lax.dot_general(
        left,
        right,
        (((1,), (1,)), ((), ())),
        precision=precision,
        preferred_element_type=jnp.float32,
    )


AXES = ("prow", "pcol")


def per_device(right_side, factor, inverses):
    block = factor.shape[1]
    rhs_width = right_side.shape[0]
    n_col = lax.axis_size("pcol")
    n_row = lax.axis_size("prow")
    steps = n_col
    row_at = lax.axis_index("prow")
    col_at = lax.axis_index("pcol")

    def at(p, c):
        return p * n_col + c

    top_rhs = right_side[:, :block]
    top_block = factor[:block]

    fetched = [top_block]
    for shift in range(1, n_col):
        pairs = [
            (at(i, j), at(i, (j + shift) % n_col))
            for i in range(1, steps)
            for j in range(i)
        ]
        fetched.append(lax.ppermute(top_block, AXES, pairs))
    fetched = jnp.stack(fetched)

    acc = jnp.zeros((rhs_width, block), jnp.float32)
    own = jnp.zeros((rhs_width, block), jnp.float32)
    for k in range(steps):
        solved = contract(top_rhs - acc, inverses[k * block : (k + 1) * block])
        own = jnp.where(row_at == k, solved, own)
        if k == steps - 1:
            break
        arrived = jnp.zeros_like(solved)
        for i in range(k + 1, steps):
            pairs = [(at(k, c), at(i, c)) for c in range(n_col)]
            arrived = arrived + lax.ppermute(solved, AXES, pairs)
        lower = lax.dynamic_index_in_dim(fetched, (col_at - k) % n_col, 0, keepdims=False)
        acc = acc + contract(arrived, lower)

    factor_later, _ = lax.optimization_barrier((factor, fetched))
    lower_second = lax.all_gather(factor_later[block:], "pcol", axis=1, tiled=True)
    lower_first = lax.all_gather(factor_later[:block], "pcol", axis=1, tiled=True)

    piece = own
    span = n_row // 2
    while span >= steps:
        pairs = [(p, p + span) for p in range(n_row) if p % (2 * span) < steps]
        arrived = lax.ppermute(piece, "prow", pairs)
        rel = row_at % (2 * span)
        piece = jnp.where((rel >= span) & (rel < span + steps), arrived, piece)
        span //= 2
    b0 = row_at % 2
    b1 = (row_at // 2) % 2
    other = lax.ppermute(piece, "prow", [(p, p ^ 2) for p in range(n_row)])
    pair = jnp.where(b1 == 0, jnp.concatenate([piece, other], axis=1), jnp.concatenate([other, piece], axis=1))
    theirs = lax.ppermute(pair, "prow", [(p, p ^ 1) for p in range(n_row)])
    mine, yours = (pair[:, :block], pair[:, block:]), (theirs[:, :block], theirs[:, block:])
    mine_first = jnp.concatenate([mine[0], yours[0], mine[1], yours[1]], axis=1)
    theirs_first = jnp.concatenate([yours[0], mine[0], yours[1], mine[1]], axis=1)
    panel = jnp.where(b0 == 0, mine_first, theirs_first)

    second = right_side[:, block:] - contract(panel, lower_second, lax.Precision.HIGH)
    first = right_side[:, :block] - contract(panel, lower_first, lax.Precision.HIGH)
    head_block = jnp.where(row_at < steps, own, first)
    return jnp.concatenate([head_block, second], axis=1)


def solution(mesh):
    return jax.shard_map(
        per_device,
        mesh=mesh,
        in_specs=(P("pcol", "prow"), P("prow", "pcol"), P()),
        out_specs=P("pcol", "prow"),
        check_vma=False,
    )
```

```python
import jax
import jax.numpy as jnp
from jax import lax
from jax.sharding import PartitionSpec as P


def contract(left, right):
    return lax.dot_general(
        left,
        right,
        (((1,), (1,)), ((), ())),
        precision=lax.Precision.HIGHEST,
        preferred_element_type=jnp.float32,
    )


AXES = ("prow", "pcol")


def per_device(right_side, factor, inverses):
    block = factor.shape[1]
    rhs_width = right_side.shape[0]
    n_col = lax.axis_size("pcol")
    n_row = lax.axis_size("prow")
    steps = n_col
    row_at = lax.axis_index("prow")
    col_at = lax.axis_index("pcol")

    def at(p, c):
        return p * n_col + c

    top_rhs = right_side[:, :block]
    top_block = factor[:block]

    fetched = [top_block]
    for shift in range(1, n_col):
        pairs = [
            (at(i, j), at(i, (j + shift) % n_col))
            for i in range(1, steps)
            for j in range(i)
        ]
        fetched.append(lax.ppermute(top_block, AXES, pairs))
    fetched = jnp.stack(fetched)

    acc = jnp.zeros((rhs_width, block), jnp.float32)
    own = jnp.zeros((rhs_width, block), jnp.float32)
    for k in range(steps):
        solved = contract(top_rhs - acc, inverses[k * block : (k + 1) * block])
        own = jnp.where(row_at == k, solved, own)
        if k == steps - 1:
            break
        arrived = jnp.zeros_like(solved)
        for i in range(k + 1, steps):
            pairs = [(at(k, c), at(i, c)) for c in range(n_col)]
            arrived = arrived + lax.ppermute(solved, AXES, pairs)
        lower = lax.dynamic_index_in_dim(fetched, (col_at - k) % n_col, 0, keepdims=False)
        acc = acc + contract(arrived, lower)

    factor_later, _ = lax.optimization_barrier((factor, fetched))
    lower_second = lax.all_gather(factor_later[block:], "pcol", axis=1, tiled=True)
    first_rows = [top_block]
    for shift in range(1, n_col):
        pairs = [
            (at(p, c), at(p, (c + shift) % n_col))
            for p in range(steps, n_row)
            for c in range(n_col)
        ]
        first_rows.append(lax.ppermute(top_block, AXES, pairs))
    first_rows = jnp.stack(first_rows)
    lower_first = jnp.concatenate(
        [
            lax.dynamic_index_in_dim(first_rows, (col_at - j) % n_col, 0, keepdims=False)
            for j in range(n_col)
        ],
        axis=1,
    )

    piece = own
    span = n_row // 2
    while span >= steps:
        pairs = [(p, p + span) for p in range(n_row) if p % (2 * span) < steps]
        arrived = lax.ppermute(piece, "prow", pairs)
        rel = row_at % (2 * span)
        piece = jnp.where((rel >= span) & (rel < span + steps), arrived, piece)
        span //= 2
    b0 = row_at % 2
    b1 = (row_at // 2) % 2
    other = lax.ppermute(piece, "prow", [(p, p ^ 2) for p in range(n_row)])
    pair = jnp.where(b1 == 0, jnp.concatenate([piece, other], axis=1), jnp.concatenate([other, piece], axis=1))
    theirs = lax.ppermute(pair, "prow", [(p, p ^ 1) for p in range(n_row)])
    mine, yours = (pair[:, :block], pair[:, block:]), (theirs[:, :block], theirs[:, block:])
    mine_first = jnp.concatenate([mine[0], yours[0], mine[1], yours[1]], axis=1)
    theirs_first = jnp.concatenate([yours[0], mine[0], yours[1], mine[1]], axis=1)
    panel = jnp.where(b0 == 0, mine_first, theirs_first)

    second = right_side[:, block:] - contract(panel, lower_second)
    first = right_side[:, :block] - contract(panel, lower_first)
    head_block = jnp.where(row_at < steps, own, first)
    return jnp.concatenate([head_block, second], axis=1)


def solution(mesh):
    return jax.shard_map(
        per_device,
        mesh=mesh,
        in_specs=(P("pcol", "prow"), P("prow", "pcol"), P()),
        out_specs=P("pcol", "prow"),
        check_vma=False,
    )
```

```python
import jax
import jax.numpy as jnp
from jax import lax
from jax.sharding import PartitionSpec as P


def contract(left, right):
    return lax.dot_general(
        left,
        right,
        (((1,), (1,)), ((), ())),
        precision=lax.Precision.HIGHEST,
        preferred_element_type=jnp.float32,
    )


AXES = ("prow", "pcol")


def per_device(right_side, factor, inverses):
    block = factor.shape[1]
    rhs_width = right_side.shape[0]
    n_col = lax.axis_size("pcol")
    n_row = lax.axis_size("prow")
    steps = n_col
    row_at = lax.axis_index("prow")
    col_at = lax.axis_index("pcol")

    def at(p, c):
        return p * n_col + c

    top_rhs = right_side[:, :block]

    lower_first = lax.all_gather(factor[:block], "pcol", axis=1, tiled=True)
    second_rows, _ = lax.optimization_barrier((factor[block:], lower_first))
    lower_second = lax.all_gather(second_rows, "pcol", axis=1, tiled=True)

    acc = jnp.zeros((rhs_width, block), jnp.float32)
    own = jnp.zeros((rhs_width, block), jnp.float32)
    for k in range(steps):
        solved = contract(top_rhs - acc, inverses[k * block : (k + 1) * block])
        own = jnp.where(row_at == k, solved, own)
        if k == steps - 1:
            break
        arrived = jnp.zeros_like(solved)
        for i in range(k + 1, steps):
            pairs = [(at(k, c), at(i, c)) for c in range(n_col)]
            arrived = arrived + lax.ppermute(solved, AXES, pairs)
        acc = acc + contract(arrived, lower_first[:, k * block : (k + 1) * block])

    piece = own
    span = n_row // 2
    while span >= steps:
        pairs = [(p, p + span) for p in range(n_row) if p % (2 * span) < steps]
        arrived = lax.ppermute(piece, "prow", pairs)
        rel = row_at % (2 * span)
        piece = jnp.where((rel >= span) & (rel < span + steps), arrived, piece)
        span //= 2
    b0 = row_at % 2
    b1 = (row_at // 2) % 2
    other = lax.ppermute(piece, "prow", [(p, p ^ 2) for p in range(n_row)])
    pair = jnp.where(b1 == 0, jnp.concatenate([piece, other], axis=1), jnp.concatenate([other, piece], axis=1))
    theirs = lax.ppermute(pair, "prow", [(p, p ^ 1) for p in range(n_row)])
    mine, yours = (pair[:, :block], pair[:, block:]), (theirs[:, :block], theirs[:, block:])
    mine_first = jnp.concatenate([mine[0], yours[0], mine[1], yours[1]], axis=1)
    theirs_first = jnp.concatenate([yours[0], mine[0], yours[1], mine[1]], axis=1)
    panel = jnp.where(b0 == 0, mine_first, theirs_first)

    second = right_side[:, block:] - contract(panel, lower_second)
    first = right_side[:, :block] - contract(panel, lower_first)
    head_block = jnp.where(row_at < steps, own, first)
    return jnp.concatenate([head_block, second], axis=1)


def solution(mesh):
    return jax.shard_map(
        per_device,
        mesh=mesh,
        in_specs=(P("pcol", "prow"), P("prow", "pcol"), P()),
        out_specs=P("pcol", "prow"),
        check_vma=False,
    )
```

```python
import jax
import jax.numpy as jnp
from jax import lax
from jax.sharding import PartitionSpec as P


def contract(left, right):
    return lax.dot_general(
        left,
        right,
        (((1,), (1,)), ((), ())),
        precision=lax.Precision.HIGHEST,
        preferred_element_type=jnp.float32,
    )


AXES = ("prow", "pcol")


def per_device(right_side, factor, inverses):
    block = factor.shape[1]
    rhs_width = right_side.shape[0]
    n_col = lax.axis_size("pcol")
    n_row = lax.axis_size("prow")
    steps = n_col
    row_at = lax.axis_index("prow")
    col_at = lax.axis_index("pcol")

    def at(p, c):
        return p * n_col + c

    top_rhs = right_side[:, :block]

    lower_first = lax.all_gather(factor[:block], "pcol", axis=1, tiled=True)
    second_rows, _ = lax.optimization_barrier((factor[block:], lower_first))
    lower_second = lax.all_gather(second_rows, "pcol", axis=1, tiled=True)

    first_rhs = top_rhs
    for i in range(1, steps):
        pairs = [(at(0, c), at(i, c)) for c in range(n_col)]
        first_rhs = jnp.where(row_at == i, lax.ppermute(top_rhs, AXES, pairs), first_rhs)

    acc = jnp.zeros((rhs_width, block), jnp.float32)
    own = jnp.zeros((rhs_width, block), jnp.float32)
    for k in range(steps):
        if k == 0:
            solved = contract(first_rhs, inverses[:block])
        else:
            solved = contract(top_rhs - acc, inverses[k * block : (k + 1) * block])
        own = jnp.where(row_at == k, solved, own)
        if k == steps - 1:
            break
        if k == 0:
            arrived = solved
        else:
            arrived = jnp.zeros_like(solved)
            for i in range(k + 1, steps):
                pairs = [(at(k, c), at(i, c)) for c in range(n_col)]
                arrived = arrived + lax.ppermute(solved, AXES, pairs)
        acc = acc + contract(arrived, lower_first[:, k * block : (k + 1) * block])

    piece = own
    span = n_row // 2
    while span >= steps:
        pairs = [(p, p + span) for p in range(n_row) if p % (2 * span) < steps]
        arrived = lax.ppermute(piece, "prow", pairs)
        rel = row_at % (2 * span)
        piece = jnp.where((rel >= span) & (rel < span + steps), arrived, piece)
        span //= 2
    b0 = row_at % 2
    b1 = (row_at // 2) % 2
    other = lax.ppermute(piece, "prow", [(p, p ^ 2) for p in range(n_row)])
    pair = jnp.where(b1 == 0, jnp.concatenate([piece, other], axis=1), jnp.concatenate([other, piece], axis=1))
    theirs = lax.ppermute(pair, "prow", [(p, p ^ 1) for p in range(n_row)])
    mine, yours = (pair[:, :block], pair[:, block:]), (theirs[:, :block], theirs[:, block:])
    mine_first = jnp.concatenate([mine[0], yours[0], mine[1], yours[1]], axis=1)
    theirs_first = jnp.concatenate([yours[0], mine[0], yours[1], mine[1]], axis=1)
    panel = jnp.where(b0 == 0, mine_first, theirs_first)

    second = right_side[:, block:] - contract(panel, lower_second)
    first = right_side[:, :block] - contract(panel, lower_first)
    head_block = jnp.where(row_at < steps, own, first)
    return jnp.concatenate([head_block, second], axis=1)


def solution(mesh):
    return jax.shard_map(
        per_device,
        mesh=mesh,
        in_specs=(P("pcol", "prow"), P("prow", "pcol"), P()),
        out_specs=P("pcol", "prow"),
        check_vma=False,
    )
```

```python
import jax
import jax.numpy as jnp
from jax import lax
from jax.sharding import PartitionSpec as P


def contract(left, right):
    return lax.dot_general(
        left,
        right,
        (((1,), (1,)), ((), ())),
        precision=lax.Precision.HIGHEST,
        preferred_element_type=jnp.float32,
    )


AXES = ("prow", "pcol")


def per_device(right_side, factor, inverses):
    block = factor.shape[1]
    rhs_width = right_side.shape[0]
    n_col = lax.axis_size("pcol")
    n_row = lax.axis_size("prow")
    steps = n_col
    row_at = lax.axis_index("prow")
    col_at = lax.axis_index("pcol")

    def at(p, c):
        return p * n_col + c

    top_rhs = right_side[:, :block]

    first_rhs = top_rhs
    for i in range(1, steps):
        pairs = [(at(0, c), at(i, c)) for c in range(n_col)]
        first_rhs = jnp.where(row_at == i, lax.ppermute(top_rhs, AXES, pairs), first_rhs)

    first_rhs, first_rows = lax.optimization_barrier((first_rhs, factor[:block]))
    lower_first = lax.all_gather(first_rows, "pcol", axis=1, tiled=True)
    second_rows, _ = lax.optimization_barrier((factor[block:], lower_first))
    lower_second = lax.all_gather(second_rows, "pcol", axis=1, tiled=True)

    acc = jnp.zeros((rhs_width, block), jnp.float32)
    own = jnp.zeros((rhs_width, block), jnp.float32)
    for k in range(steps):
        if k == 0:
            solved = contract(first_rhs, inverses[:block])
        else:
            solved = contract(top_rhs - acc, inverses[k * block : (k + 1) * block])
        own = jnp.where(row_at == k, solved, own)
        if k == steps - 1:
            break
        if k == 0:
            arrived = solved
        else:
            arrived = jnp.zeros_like(solved)
            for i in range(k + 1, steps):
                pairs = [(at(k, c), at(i, c)) for c in range(n_col)]
                arrived = arrived + lax.ppermute(solved, AXES, pairs)
        acc = acc + contract(arrived, lower_first[:, k * block : (k + 1) * block])

    piece = own
    span = n_row // 2
    while span >= steps:
        pairs = [(p, p + span) for p in range(n_row) if p % (2 * span) < steps]
        arrived = lax.ppermute(piece, "prow", pairs)
        rel = row_at % (2 * span)
        piece = jnp.where((rel >= span) & (rel < span + steps), arrived, piece)
        span //= 2
    b0 = row_at % 2
    b1 = (row_at // 2) % 2
    other = lax.ppermute(piece, "prow", [(p, p ^ 2) for p in range(n_row)])
    pair = jnp.where(b1 == 0, jnp.concatenate([piece, other], axis=1), jnp.concatenate([other, piece], axis=1))
    theirs = lax.ppermute(pair, "prow", [(p, p ^ 1) for p in range(n_row)])
    mine, yours = (pair[:, :block], pair[:, block:]), (theirs[:, :block], theirs[:, block:])
    mine_first = jnp.concatenate([mine[0], yours[0], mine[1], yours[1]], axis=1)
    theirs_first = jnp.concatenate([yours[0], mine[0], yours[1], mine[1]], axis=1)
    panel = jnp.where(b0 == 0, mine_first, theirs_first)

    second = right_side[:, block:] - contract(panel, lower_second)
    first = right_side[:, :block] - contract(panel, lower_first)
    head_block = jnp.where(row_at < steps, own, first)
    return jnp.concatenate([head_block, second], axis=1)


def solution(mesh):
    return jax.shard_map(
        per_device,
        mesh=mesh,
        in_specs=(P("pcol", "prow"), P("prow", "pcol"), P()),
        out_specs=P("pcol", "prow"),
        check_vma=False,
    )
```

```python
import jax
import jax.numpy as jnp
from jax import lax
from jax.sharding import PartitionSpec as P


def contract(left, right):
    return lax.dot_general(
        left,
        right,
        (((1,), (1,)), ((), ())),
        precision=lax.Precision.HIGHEST,
        preferred_element_type=jnp.float32,
    )


AXES = ("prow", "pcol")


def per_device(right_side, factor, inverses):
    block = factor.shape[1]
    rhs_width = right_side.shape[0]
    n_col = lax.axis_size("pcol")
    n_row = lax.axis_size("prow")
    steps = n_col
    row_at = lax.axis_index("prow")
    col_at = lax.axis_index("pcol")

    def at(p, c):
        return p * n_col + c

    top_rhs = right_side[:, :block]

    first_rhs = top_rhs
    for i in range(1, steps):
        pairs = [(at(0, c), at(i, c)) for c in range(n_col)]
        first_rhs = jnp.where(row_at == i, lax.ppermute(top_rhs, AXES, pairs), first_rhs)

    first_rhs, first_rows = lax.optimization_barrier((first_rhs, factor[:block]))
    lower_first = lax.all_to_all(jnp.tile(first_rows, (1, 4)), "pcol", 1, 1, tiled=True)
    second_rows, _ = lax.optimization_barrier((factor[block:], lower_first))
    lower_second = lax.all_to_all(jnp.tile(second_rows, (1, 4)), "pcol", 1, 1, tiled=True)

    acc = jnp.zeros((rhs_width, block), jnp.float32)
    own = jnp.zeros((rhs_width, block), jnp.float32)
    for k in range(steps):
        if k == 0:
            solved = contract(first_rhs, inverses[:block])
        else:
            solved = contract(top_rhs - acc, inverses[k * block : (k + 1) * block])
        own = jnp.where(row_at == k, solved, own)
        if k == steps - 1:
            break
        if k == 0:
            arrived = solved
        else:
            arrived = jnp.zeros_like(solved)
            for i in range(k + 1, steps):
                pairs = [(at(k, c), at(i, c)) for c in range(n_col)]
                arrived = arrived + lax.ppermute(solved, AXES, pairs)
        acc = acc + contract(arrived, lower_first[:, k * block : (k + 1) * block])

    piece = own
    span = n_row // 2
    while span >= steps:
        pairs = [(p, p + span) for p in range(n_row) if p % (2 * span) < steps]
        arrived = lax.ppermute(piece, "prow", pairs)
        rel = row_at % (2 * span)
        piece = jnp.where((rel >= span) & (rel < span + steps), arrived, piece)
        span //= 2
    b0 = row_at % 2
    b1 = (row_at // 2) % 2
    other = lax.ppermute(piece, "prow", [(p, p ^ 2) for p in range(n_row)])
    pair = jnp.where(b1 == 0, jnp.concatenate([piece, other], axis=1), jnp.concatenate([other, piece], axis=1))
    theirs = lax.ppermute(pair, "prow", [(p, p ^ 1) for p in range(n_row)])
    mine, yours = (pair[:, :block], pair[:, block:]), (theirs[:, :block], theirs[:, block:])
    mine_first = jnp.concatenate([mine[0], yours[0], mine[1], yours[1]], axis=1)
    theirs_first = jnp.concatenate([yours[0], mine[0], yours[1], mine[1]], axis=1)
    panel = jnp.where(b0 == 0, mine_first, theirs_first)

    second = right_side[:, block:] - contract(panel, lower_second)
    first = right_side[:, :block] - contract(panel, lower_first)
    head_block = jnp.where(row_at < steps, own, first)
    return jnp.concatenate([head_block, second], axis=1)


def solution(mesh):
    return jax.shard_map(
        per_device,
        mesh=mesh,
        in_specs=(P("pcol", "prow"), P("prow", "pcol"), P()),
        out_specs=P("pcol", "prow"),
        check_vma=False,
    )
```

```python
import jax
import jax.numpy as jnp
from jax import lax
from jax.sharding import PartitionSpec as P


def contract(left, right):
    return lax.dot_general(
        left,
        right,
        (((1,), (1,)), ((), ())),
        precision=lax.Precision.HIGHEST,
        preferred_element_type=jnp.float32,
    )


AXES = ("prow", "pcol")


def per_device(right_side, factor, inverses):
    block = factor.shape[1]
    rhs_width = right_side.shape[0]
    n_col = lax.axis_size("pcol")
    n_row = lax.axis_size("prow")
    steps = n_col
    row_at = lax.axis_index("prow")
    col_at = lax.axis_index("pcol")

    def at(p, c):
        return p * n_col + c

    top_rhs = right_side[:, :block]

    first_rhs = top_rhs
    for i in range(1, steps):
        pairs = [(at(0, c), at(i, c)) for c in range(n_col)]
        first_rhs = jnp.where(row_at == i, lax.ppermute(top_rhs, AXES, pairs), first_rhs)

    first_rhs, first_rows = lax.optimization_barrier((first_rhs, factor[:block]))
    lower_first = lax.all_gather(first_rows, "pcol", axis=1, tiled=True)
    second_rows, _ = lax.optimization_barrier((factor[block:], lower_first))
    lower_second = lax.all_gather(second_rows, "pcol", axis=1, tiled=True)

    acc = jnp.zeros((rhs_width, block), jnp.float32)
    own = jnp.zeros((rhs_width, block), jnp.float32)
    for k in range(steps):
        if k == 0:
            solved = contract(first_rhs, inverses[:block])
        else:
            solved = contract(top_rhs - acc, inverses[k * block : (k + 1) * block])
        own = jnp.where(row_at == k, solved, own)
        if k == steps - 1:
            break
        if k == 0:
            arrived = solved
        else:
            arrived = jnp.zeros_like(solved)
            for i in range(k + 1, steps):
                pairs = [(at(k, c), at(i, c)) for c in range(n_col)]
                arrived = arrived + lax.ppermute(solved, AXES, pairs)
        acc = acc + contract(arrived, lower_first[:, k * block : (k + 1) * block])

    piece = own
    fan_z = min(steps, n_row // steps)
    stride_x = steps * fan_z
    for stride, fan in ((stride_x, n_row // stride_x), (steps, fan_z)):
        holders = [p for p in range(n_row) if p % (stride * fan) < steps]
        received = piece
        for hop in range(1, fan):
            pairs = [(p, p + hop * stride) for p in holders]
            arrived = lax.ppermute(piece, "prow", pairs)
            received = jnp.where((row_at % (stride * fan)) // stride == hop, arrived, received)
        piece = jnp.where(row_at % stride < steps, received, piece)
    b0 = row_at % 2
    b1 = (row_at // 2) % 2
    other = lax.ppermute(piece, "prow", [(p, p ^ 2) for p in range(n_row)])
    pair = jnp.where(b1 == 0, jnp.concatenate([piece, other], axis=1), jnp.concatenate([other, piece], axis=1))
    theirs = lax.ppermute(pair, "prow", [(p, p ^ 1) for p in range(n_row)])
    mine, yours = (pair[:, :block], pair[:, block:]), (theirs[:, :block], theirs[:, block:])
    mine_first = jnp.concatenate([mine[0], yours[0], mine[1], yours[1]], axis=1)
    theirs_first = jnp.concatenate([yours[0], mine[0], yours[1], mine[1]], axis=1)
    panel = jnp.where(b0 == 0, mine_first, theirs_first)

    second = right_side[:, block:] - contract(panel, lower_second)
    first = right_side[:, :block] - contract(panel, lower_first)
    head_block = jnp.where(row_at < steps, own, first)
    return jnp.concatenate([head_block, second], axis=1)


def solution(mesh):
    return jax.shard_map(
        per_device,
        mesh=mesh,
        in_specs=(P("pcol", "prow"), P("prow", "pcol"), P()),
        out_specs=P("pcol", "prow"),
        check_vma=False,
    )
```

```python
import jax
import jax.numpy as jnp
from jax import lax
from jax.sharding import PartitionSpec as P


def contract(left, right):
    return lax.dot_general(
        left,
        right,
        (((1,), (1,)), ((), ())),
        precision=lax.Precision.HIGHEST,
        preferred_element_type=jnp.float32,
    )


AXES = ("prow", "pcol")


def per_device(right_side, factor, inverses):
    block = factor.shape[1]
    rhs_width = right_side.shape[0]
    n_col = lax.axis_size("pcol")
    n_row = lax.axis_size("prow")
    steps = n_col
    row_at = lax.axis_index("prow")
    col_at = lax.axis_index("pcol")

    def at(p, c):
        return p * n_col + c

    top_rhs = right_side[:, :block]

    first_rhs = top_rhs
    for i in range(1, steps):
        pairs = [(at(0, c), at(i, c)) for c in range(n_col)]
        first_rhs = jnp.where(row_at == i, lax.ppermute(top_rhs, AXES, pairs), first_rhs)

    first_rhs, first_rows = lax.optimization_barrier((first_rhs, factor[:block]))
    lower_first = lax.all_gather(first_rows, "pcol", axis=1, tiled=True)
    second_rows, _ = lax.optimization_barrier((factor[block:], lower_first))
    lower_second = lax.all_gather(second_rows, "pcol", axis=1, tiled=True)

    acc = jnp.zeros((rhs_width, block), jnp.float32)
    own = jnp.zeros((rhs_width, block), jnp.float32)
    for k in range(steps):
        if k == 0:
            solved = contract(first_rhs, inverses[:block])
        else:
            solved = contract(top_rhs - acc, inverses[k * block : (k + 1) * block])
        own = jnp.where(row_at == k, solved, own)
        if k == steps - 1:
            break
        if k == 0:
            arrived = solved
        else:
            arrived = jnp.zeros_like(solved)
            for i in range(k + 1, steps):
                pairs = [(at(k, c), at(i, c)) for c in range(n_col)]
                arrived = arrived + lax.ppermute(solved, AXES, pairs)
        acc = acc + contract(arrived, lower_first[:, k * block : (k + 1) * block])

    piece = own
    fan_z = min(steps, n_row // steps)
    stride_x = steps * fan_z
    for stride, fan in ((stride_x, n_row // stride_x), (steps, fan_z)):
        holders = [p for p in range(n_row) if p % (stride * fan) < steps]
        received = piece
        for hop in range(1, fan):
            pairs = [(p, p + hop * stride) for p in holders]
            arrived = lax.ppermute(piece, "prow", pairs)
            received = jnp.where((row_at % (stride * fan)) // stride == hop, arrived, received)
        piece = jnp.where(row_at % stride < steps, received, piece)
    b0 = row_at % 2
    b1 = (row_at // 2) % 2
    other = lax.ppermute(piece, "prow", [(p, p ^ 2) for p in range(n_row)])
    pair = jnp.where(b1 == 0, jnp.concatenate([piece, other], axis=1), jnp.concatenate([other, piece], axis=1))
    theirs = lax.ppermute(pair, "prow", [(p, p ^ 1) for p in range(n_row)])
    mine, yours = (pair[:, :block], pair[:, block:]), (theirs[:, :block], theirs[:, block:])
    mine_first = jnp.concatenate([mine[0], yours[0], mine[1], yours[1]], axis=1)
    theirs_first = jnp.concatenate([yours[0], mine[0], yours[1], mine[1]], axis=1)
    panel = jnp.where(b0 == 0, mine_first, theirs_first)

    def parts(value):
        high = lax.reduce_precision(value, exponent_bits=8, mantissa_bits=7)
        rest = value - high
        middle = lax.reduce_precision(rest, exponent_bits=8, mantissa_bits=7)
        low = rest - middle
        return [part.astype(jnp.bfloat16) for part in (high, middle, low)]

    panel_parts = parts(panel)

    def product(lower):
        lower_parts = parts(lower)
        total = None
        for i, j in ((2, 0), (1, 1), (0, 2), (1, 0), (0, 1), (0, 0)):
            term = lax.dot_general(
                panel_parts[i], lower_parts[j], (((1,), (1,)), ((), ())),
                preferred_element_type=jnp.float32,
            )
            total = term if total is None else total + term
        return total

    second = right_side[:, block:] - product(lower_second)
    first = right_side[:, :block] - product(lower_first)
    head_block = jnp.where(row_at < steps, own, first)
    return jnp.concatenate([head_block, second], axis=1)


def solution(mesh):
    return jax.shard_map(
        per_device,
        mesh=mesh,
        in_specs=(P("pcol", "prow"), P("prow", "pcol"), P()),
        out_specs=P("pcol", "prow"),
        check_vma=False,
    )
```

```python
import jax
import jax.numpy as jnp
from jax import lax
from jax.sharding import PartitionSpec as P


def contract(left, right):
    return lax.dot_general(
        left,
        right,
        (((1,), (1,)), ((), ())),
        precision=lax.Precision.HIGHEST,
        preferred_element_type=jnp.float32,
    )


AXES = ("prow", "pcol")


def per_device(right_side, factor, inverses):
    block = factor.shape[1]
    rhs_width = right_side.shape[0]
    n_col = lax.axis_size("pcol")
    n_row = lax.axis_size("prow")
    steps = n_col
    row_at = lax.axis_index("prow")
    col_at = lax.axis_index("pcol")

    def at(p, c):
        return p * n_col + c

    top_rhs = right_side[:, :block]

    first_rhs = top_rhs
    for i in range(1, steps):
        pairs = [(at(0, c), at(i, c)) for c in range(n_col)]
        first_rhs = jnp.where(row_at == i, lax.ppermute(top_rhs, AXES, pairs), first_rhs)

    first_rhs, first_rows = lax.optimization_barrier((first_rhs, factor[:block]))
    lower_first = lax.all_gather(first_rows, "pcol", axis=1, tiled=True)
    second_rows, _ = lax.optimization_barrier((factor[block:], lower_first))
    lower_second = lax.all_gather(second_rows, "pcol", axis=1, tiled=True)

    acc = jnp.zeros((rhs_width, block), jnp.float32)
    own = jnp.zeros((rhs_width, block), jnp.float32)
    for k in range(steps):
        if k == 0:
            solved = contract(first_rhs, inverses[:block])
        else:
            solved = contract(top_rhs - acc, inverses[k * block : (k + 1) * block])
        own = jnp.where(row_at == k, solved, own)
        if k == steps - 1:
            break
        if k == 0:
            arrived = solved
        else:
            arrived = jnp.zeros_like(solved)
            for i in range(k + 1, steps):
                pairs = [(at(k, c), at(i, c)) for c in range(n_col)]
                arrived = arrived + lax.ppermute(solved, AXES, pairs)
        acc = acc + contract(arrived, lower_first[:, k * block : (k + 1) * block])

    def parts(value):
        high = lax.reduce_precision(value, exponent_bits=8, mantissa_bits=7)
        rest = value - high
        middle = lax.reduce_precision(rest, exponent_bits=8, mantissa_bits=7)
        low = rest - middle
        return [part.astype(jnp.bfloat16) for part in (high, middle, low)]

    first_parts, piece = lax.optimization_barrier((parts(lower_first), own))
    fan_z = min(steps, n_row // steps)
    stride_x = steps * fan_z
    for stride, fan in ((stride_x, n_row // stride_x), (steps, fan_z)):
        holders = [p for p in range(n_row) if p % (stride * fan) < steps]
        received = piece
        for hop in range(1, fan):
            pairs = [(p, p + hop * stride) for p in holders]
            arrived = lax.ppermute(piece, "prow", pairs)
            received = jnp.where((row_at % (stride * fan)) // stride == hop, arrived, received)
        piece = jnp.where(row_at % stride < steps, received, piece)
    second_parts, piece = lax.optimization_barrier((parts(lower_second), piece))
    b0 = row_at % 2
    b1 = (row_at // 2) % 2
    other = lax.ppermute(piece, "prow", [(p, p ^ 2) for p in range(n_row)])
    pair = jnp.where(b1 == 0, jnp.concatenate([piece, other], axis=1), jnp.concatenate([other, piece], axis=1))
    theirs = lax.ppermute(pair, "prow", [(p, p ^ 1) for p in range(n_row)])
    mine, yours = (pair[:, :block], pair[:, block:]), (theirs[:, :block], theirs[:, block:])
    mine_first = jnp.concatenate([mine[0], yours[0], mine[1], yours[1]], axis=1)
    theirs_first = jnp.concatenate([yours[0], mine[0], yours[1], mine[1]], axis=1)
    panel = jnp.where(b0 == 0, mine_first, theirs_first)

    panel_parts = parts(panel)

    def product(lower_parts):
        total = None
        for i, j in ((2, 0), (1, 1), (0, 2), (1, 0), (0, 1), (0, 0)):
            term = lax.dot_general(
                panel_parts[i], lower_parts[j], (((1,), (1,)), ((), ())),
                preferred_element_type=jnp.float32,
            )
            total = term if total is None else total + term
        return total

    second = right_side[:, block:] - product(second_parts)
    first = right_side[:, :block] - product(first_parts)
    head_block = jnp.where(row_at < steps, own, first)
    return jnp.concatenate([head_block, second], axis=1)


def solution(mesh):
    return jax.shard_map(
        per_device,
        mesh=mesh,
        in_specs=(P("pcol", "prow"), P("prow", "pcol"), P()),
        out_specs=P("pcol", "prow"),
        check_vma=False,
    )
```

```python
import jax
import jax.numpy as jnp
from jax import lax
from jax.sharding import PartitionSpec as P


def contract(left, right):
    return lax.dot_general(
        left,
        right,
        (((1,), (1,)), ((), ())),
        precision=lax.Precision.HIGHEST,
        preferred_element_type=jnp.float32,
    )


AXES = ("prow", "pcol")


def per_device(right_side, factor, inverses):
    block = factor.shape[1]
    rhs_width = right_side.shape[0]
    n_col = lax.axis_size("pcol")
    n_row = lax.axis_size("prow")
    steps = n_col
    row_at = lax.axis_index("prow")
    col_at = lax.axis_index("pcol")

    def at(p, c):
        return p * n_col + c

    top_rhs = right_side[:, :block]

    first_rhs = top_rhs
    for i in range(1, steps):
        pairs = [(at(0, c), at(i, c)) for c in range(n_col)]
        first_rhs = jnp.where(row_at == i, lax.ppermute(top_rhs, AXES, pairs), first_rhs)

    first_rhs, first_rows = lax.optimization_barrier((first_rhs, factor[:block]))
    lower_first = lax.all_gather(first_rows, "pcol", axis=1, tiled=True)
    second_rows, _ = lax.optimization_barrier((factor[block:], lower_first))
    lower_second = lax.all_gather(second_rows, "pcol", axis=1, tiled=True)

    acc = jnp.zeros((rhs_width, block), jnp.float32)
    own = jnp.zeros((rhs_width, block), jnp.float32)
    for k in range(steps):
        if k == 0:
            solved = contract(first_rhs, inverses[:block])
        else:
            solved = contract(top_rhs - acc, inverses[k * block : (k + 1) * block])
        own = jnp.where(row_at == k, solved, own)
        if k == steps - 2:
            own_early = own
        if k == steps - 1:
            break
        if k == 0:
            arrived = solved
        else:
            arrived = jnp.zeros_like(solved)
            for i in range(k + 1, steps):
                pairs = [(at(k, c), at(i, c)) for c in range(n_col)]
                arrived = arrived + lax.ppermute(solved, AXES, pairs)
        acc = acc + contract(arrived, lower_first[:, k * block : (k + 1) * block])

    fan_z = min(steps, n_row // steps)
    stride_x = steps * fan_z
    spread = []
    for piece, sources in ((own_early, range(steps - 1)), (own, (steps - 1,))):
        for stride, fan in ((stride_x, n_row // stride_x), (steps, fan_z)):
            holders = [p for p in range(n_row) if p % (stride * fan) in sources]
            received = piece
            for hop in range(1, fan):
                pairs = [(p, p + hop * stride) for p in holders]
                arrived = lax.ppermute(piece, "prow", pairs)
                received = jnp.where((row_at % (stride * fan)) // stride == hop, arrived, received)
            piece = jnp.where(row_at % stride < steps, received, piece)
        spread.append(piece)
    piece = jnp.where(row_at % steps == steps - 1, spread[1], spread[0])
    b0 = row_at % 2
    b1 = (row_at // 2) % 2
    other = lax.ppermute(piece, "prow", [(p, p ^ 2) for p in range(n_row)])
    pair = jnp.where(b1 == 0, jnp.concatenate([piece, other], axis=1), jnp.concatenate([other, piece], axis=1))
    theirs = lax.ppermute(pair, "prow", [(p, p ^ 1) for p in range(n_row)])
    mine, yours = (pair[:, :block], pair[:, block:]), (theirs[:, :block], theirs[:, block:])
    mine_first = jnp.concatenate([mine[0], yours[0], mine[1], yours[1]], axis=1)
    theirs_first = jnp.concatenate([yours[0], mine[0], yours[1], mine[1]], axis=1)
    panel = jnp.where(b0 == 0, mine_first, theirs_first)

    second = right_side[:, block:] - contract(panel, lower_second)
    first = right_side[:, :block] - contract(panel, lower_first)
    head_block = jnp.where(row_at < steps, own, first)
    return jnp.concatenate([head_block, second], axis=1)


def solution(mesh):
    return jax.shard_map(
        per_device,
        mesh=mesh,
        in_specs=(P("pcol", "prow"), P("prow", "pcol"), P()),
        out_specs=P("pcol", "prow"),
        check_vma=False,
    )
```

```python
import jax
import jax.numpy as jnp
from jax import lax
from jax.sharding import PartitionSpec as P


def contract(left, right):
    return lax.dot_general(
        left,
        right,
        (((1,), (1,)), ((), ())),
        precision=lax.Precision.HIGHEST,
        preferred_element_type=jnp.float32,
    )


AXES = ("prow", "pcol")


def per_device(right_side, factor, inverses):
    block = factor.shape[1]
    rhs_width = right_side.shape[0]
    n_col = lax.axis_size("pcol")
    n_row = lax.axis_size("prow")
    steps = n_col
    row_at = lax.axis_index("prow")
    col_at = lax.axis_index("pcol")

    def at(p, c):
        return p * n_col + c

    top_rhs = right_side[:, :block]

    first_rhs = top_rhs
    for i in range(1, steps):
        pairs = [(at(0, c), at(i, c)) for c in range(n_col)]
        first_rhs = jnp.where(row_at == i, lax.ppermute(top_rhs, AXES, pairs), first_rhs)

    first_rhs, first_rows = lax.optimization_barrier((first_rhs, factor[:block]))
    lower_first = lax.all_gather(first_rows, "pcol", axis=1, tiled=True)
    second_rows, _ = lax.optimization_barrier((factor[block:], lower_first))
    lower_second = lax.all_gather(second_rows, "pcol", axis=1, tiled=True)

    acc = jnp.zeros((rhs_width, block), jnp.float32)
    own = jnp.zeros((rhs_width, block), jnp.float32)
    for k in range(steps):
        if k == 0:
            solved = contract(first_rhs, inverses[:block])
        else:
            solved = contract(top_rhs - acc, inverses[k * block : (k + 1) * block])
        own = jnp.where(row_at == k, solved, own)
        if k == steps - 2:
            own_early = own
        if k == steps - 1:
            break
        if k == 0:
            arrived = solved
        else:
            arrived = jnp.zeros_like(solved)
            for i in range(k + 1, steps):
                pairs = [(at(k, c), at(i, c)) for c in range(n_col)]
                arrived = arrived + lax.ppermute(solved, AXES, pairs)
        acc = acc + contract(arrived, lower_first[:, k * block : (k + 1) * block])

    fan_z = min(steps, n_row // steps)
    stride_x = steps * fan_z
    spread = []
    for piece, sources in ((own_early, range(steps - 1)), (own, (steps - 1,))):
        for stride, fan in ((stride_x, n_row // stride_x), (steps, fan_z)):
            holders = [p for p in range(n_row) if p % (stride * fan) in sources]
            received = piece
            for hop in range(1, fan):
                pairs = [(p, p + hop * stride) for p in holders]
                arrived = lax.ppermute(piece, "prow", pairs)
                received = jnp.where((row_at % (stride * fan)) // stride == hop, arrived, received)
            piece = jnp.where(row_at % stride < steps, received, piece)
        spread.append(piece)
    piece = spread[0]
    b0 = row_at % 2
    b1 = (row_at // 2) % 2
    other = lax.ppermute(piece, "prow", [(p, p ^ 2) for p in range(n_row)])
    pair = jnp.where(b1 == 0, jnp.concatenate([piece, other], axis=1), jnp.concatenate([other, piece], axis=1))
    theirs = lax.ppermute(pair, "prow", [(p, p ^ 1) for p in range(n_row)])
    mine, yours = (pair[:, :block], pair[:, block:]), (theirs[:, :block], theirs[:, block:])
    mine_first = jnp.concatenate([mine[0], yours[0], mine[1], yours[1]], axis=1)
    theirs_first = jnp.concatenate([yours[0], mine[0], yours[1], mine[1]], axis=1)
    panel = jnp.where(b0 == 0, mine_first, theirs_first)
    last = jnp.where(row_at % steps == steps - 1, spread[1], jnp.zeros_like(spread[1]))
    for mask in range(1, steps):
        pairs = [(p, p ^ mask) for p in range(n_row) if p % steps == steps - 1]
        last = last + lax.ppermute(spread[1], "prow", pairs)
    last_cols = slice((steps - 1) * block, steps * block)

    second = right_side[:, block:] - (
        contract(panel, lower_second) + contract(last, lower_second[:, last_cols])
    )
    first = right_side[:, :block] - (
        contract(panel, lower_first) + contract(last, lower_first[:, last_cols])
    )
    head_block = jnp.where(row_at < steps, own, first)
    return jnp.concatenate([head_block, second], axis=1)


def solution(mesh):
    return jax.shard_map(
        per_device,
        mesh=mesh,
        in_specs=(P("pcol", "prow"), P("prow", "pcol"), P()),
        out_specs=P("pcol", "prow"),
        check_vma=False,
    )
```

```python
import jax
import jax.numpy as jnp
from jax import lax
from jax.sharding import PartitionSpec as P


def contract(left, right):
    return lax.dot_general(
        left,
        right,
        (((1,), (1,)), ((), ())),
        precision=lax.Precision.HIGHEST,
        preferred_element_type=jnp.float32,
    )


AXES = ("prow", "pcol")


def per_device(right_side, factor, inverses):
    block = factor.shape[1]
    rhs_width = right_side.shape[0]
    n_col = lax.axis_size("pcol")
    n_row = lax.axis_size("prow")
    steps = n_col
    row_at = lax.axis_index("prow")
    col_at = lax.axis_index("pcol")

    def at(p, c):
        return p * n_col + c

    top_rhs = right_side[:, :block]

    first_rhs = top_rhs
    for i in range(1, steps):
        pairs = [(at(0, c), at(i, c)) for c in range(n_col)]
        first_rhs = jnp.where(row_at == i, lax.ppermute(top_rhs, AXES, pairs), first_rhs)

    first_rhs, first_rows = lax.optimization_barrier((first_rhs, factor[:block]))
    lower_first = lax.all_gather(first_rows, "pcol", axis=1, tiled=True)
    second_rows, _ = lax.optimization_barrier((factor[block:], lower_first))
    lower_second = lax.all_gather(second_rows, "pcol", axis=1, tiled=True)

    acc = jnp.zeros((rhs_width, block), jnp.float32)
    own = jnp.zeros((rhs_width, block), jnp.float32)
    for k in range(steps):
        if k == 0:
            solved = contract(first_rhs, inverses[:block])
        else:
            solved = contract(top_rhs - acc, inverses[k * block : (k + 1) * block])
        own = jnp.where(row_at == k, solved, own)
        if k == steps - 2:
            own_early = own
        if k == steps - 1:
            break
        if k == 0:
            arrived = solved
        else:
            arrived = jnp.zeros_like(solved)
            for i in range(k + 1, steps):
                pairs = [(at(k, c), at(i, c)) for c in range(n_col)]
                arrived = arrived + lax.ppermute(solved, AXES, pairs)
        acc = acc + contract(arrived, lower_first[:, k * block : (k + 1) * block])

    fan_z = min(steps, n_row // steps)
    stride_x = steps * fan_z
    spread = []
    for piece, sources in ((own_early, range(steps - 1)), (own, (steps - 1,))):
        for stride, fan in ((stride_x, n_row // stride_x), (steps, fan_z)):
            holders = [p for p in range(n_row) if p % (stride * fan) in sources]
            received = piece
            for hop in sorted(range(1, fan), key=lambda h: -min(h, fan - h)):
                pairs = [(p, p + hop * stride) for p in holders]
                arrived = lax.ppermute(piece, "prow", pairs)
                received = jnp.where((row_at % (stride * fan)) // stride == hop, arrived, received)
            piece = jnp.where(row_at % stride < steps, received, piece)
        spread.append(piece)
    piece = jnp.where(row_at % steps == steps - 1, spread[1], spread[0])
    b0 = row_at % 2
    b1 = (row_at // 2) % 2
    other = lax.ppermute(piece, "prow", [(p, p ^ 2) for p in range(n_row)])
    pair = jnp.where(b1 == 0, jnp.concatenate([piece, other], axis=1), jnp.concatenate([other, piece], axis=1))
    theirs = lax.ppermute(pair, "prow", [(p, p ^ 1) for p in range(n_row)])
    mine, yours = (pair[:, :block], pair[:, block:]), (theirs[:, :block], theirs[:, block:])
    mine_first = jnp.concatenate([mine[0], yours[0], mine[1], yours[1]], axis=1)
    theirs_first = jnp.concatenate([yours[0], mine[0], yours[1], mine[1]], axis=1)
    panel = jnp.where(b0 == 0, mine_first, theirs_first)

    second = right_side[:, block:] - contract(panel, lower_second)
    first = right_side[:, :block] - contract(panel, lower_first)
    head_block = jnp.where(row_at < steps, own, first)
    return jnp.concatenate([head_block, second], axis=1)


def solution(mesh):
    return jax.shard_map(
        per_device,
        mesh=mesh,
        in_specs=(P("pcol", "prow"), P("prow", "pcol"), P()),
        out_specs=P("pcol", "prow"),
        check_vma=False,
    )
```

```python
import jax
import jax.numpy as jnp
from jax import lax
from jax.sharding import PartitionSpec as P


def contract(left, right):
    return lax.dot_general(
        left,
        right,
        (((1,), (1,)), ((), ())),
        precision=lax.Precision.HIGHEST,
        preferred_element_type=jnp.float32,
    )


AXES = ("prow", "pcol")


def per_device(right_side, factor, inverses):
    block = factor.shape[1]
    rhs_width = right_side.shape[0]
    n_col = lax.axis_size("pcol")
    n_row = lax.axis_size("prow")
    steps = n_col
    row_at = lax.axis_index("prow")
    col_at = lax.axis_index("pcol")

    def at(p, c):
        return p * n_col + c

    top_rhs = right_side[:, :block]

    first_rhs = top_rhs
    for i in range(1, steps):
        pairs = [(at(0, c), at(i, c)) for c in range(n_col)]
        first_rhs = jnp.where(row_at == i, lax.ppermute(top_rhs, AXES, pairs), first_rhs)

    first_rhs, first_rows = lax.optimization_barrier((first_rhs, factor[:block]))
    lower_first = lax.all_gather(first_rows, "pcol", axis=1, tiled=True)
    second_rows, _ = lax.optimization_barrier((factor[block:], lower_first))
    lower_second = lax.all_gather(second_rows, "pcol", axis=1, tiled=True)

    acc = jnp.zeros((rhs_width, block), jnp.float32)
    own = jnp.zeros((rhs_width, block), jnp.float32)
    for k in range(steps):
        if k == 0:
            solved = contract(first_rhs, inverses[:block])
        else:
            solved = contract(top_rhs - acc, inverses[k * block : (k + 1) * block])
        own = jnp.where(row_at == k, solved, own)
        if k == steps - 2:
            own_early = own
        if k == steps - 1:
            break
        if k == 0:
            arrived = solved
        else:
            arrived = jnp.zeros_like(solved)
            for i in range(k + 1, steps):
                pairs = [(at(k, c), at(i, c)) for c in range(n_col)]
                arrived = arrived + lax.ppermute(solved, AXES, pairs)
        acc = acc + contract(arrived, lower_first[:, k * block : (k + 1) * block])

    fan_z = min(steps, n_row // steps)
    stride_x = steps * fan_z
    spread = []
    for piece, sources in ((own_early, range(steps - 1)), (own, (steps - 1,))):
        for stride, fan in ((stride_x, n_row // stride_x), (steps, fan_z)):
            holders = [p for p in range(n_row) if p % (stride * fan) in sources]
            received = piece
            for hop in range(1, fan):
                pairs = [(p, p + hop * stride) for p in holders]
                arrived = lax.ppermute(piece, "prow", pairs)
                received = jnp.where((row_at % (stride * fan)) // stride == hop, arrived, received)
            piece = jnp.where(row_at % stride < steps, received, piece)
        spread.append(piece)
    piece = spread[0]
    b0 = row_at % 2
    b1 = (row_at // 2) % 2
    other = lax.ppermute(piece, "prow", [(p, p ^ 2) for p in range(n_row)])
    pair = jnp.where(b1 == 0, jnp.concatenate([piece, other], axis=1), jnp.concatenate([other, piece], axis=1))
    theirs = lax.ppermute(pair, "prow", [(p, p ^ 1) for p in range(n_row)])
    mine, yours = (pair[:, :block], pair[:, block:]), (theirs[:, :block], theirs[:, block:])
    mine_first = jnp.concatenate([mine[0], yours[0], mine[1]], axis=1)
    theirs_first = jnp.concatenate([yours[0], mine[0], yours[1]], axis=1)
    last = jnp.where(row_at % steps == steps - 1, spread[1], jnp.zeros_like(spread[1]))
    for mask in range(1, steps):
        pairs = [(p, p ^ mask) for p in range(n_row) if p % steps == steps - 1]
        last = last + lax.ppermute(spread[1], "prow", pairs)
    panel = jnp.concatenate([jnp.where(b0 == 0, mine_first, theirs_first), last], axis=1)

    second = right_side[:, block:] - contract(panel, lower_second)
    first = right_side[:, :block] - contract(panel, lower_first)
    head_block = jnp.where(row_at < steps, own, first)
    return jnp.concatenate([head_block, second], axis=1)


def solution(mesh):
    return jax.shard_map(
        per_device,
        mesh=mesh,
        in_specs=(P("pcol", "prow"), P("prow", "pcol"), P()),
        out_specs=P("pcol", "prow"),
        check_vma=False,
    )
```

```python
import jax
import jax.numpy as jnp
from jax import lax
from jax.sharding import PartitionSpec as P


def contract(left, right):
    return lax.dot_general(
        left,
        right,
        (((1,), (1,)), ((), ())),
        precision=lax.Precision.HIGHEST,
        preferred_element_type=jnp.float32,
    )


AXES = ("prow", "pcol")


def per_device(right_side, factor, inverses):
    block = factor.shape[1]
    rhs_width = right_side.shape[0]
    n_col = lax.axis_size("pcol")
    n_row = lax.axis_size("prow")
    steps = n_col
    row_at = lax.axis_index("prow")
    col_at = lax.axis_index("pcol")

    def at(p, c):
        return p * n_col + c

    top_rhs = right_side[:, :block]

    first_rhs = top_rhs
    for i in range(1, steps):
        pairs = [(at(0, c), at(i, c)) for c in range(n_col)]
        first_rhs = jnp.where(row_at == i, lax.ppermute(top_rhs, AXES, pairs), first_rhs)

    first_rhs, first_rows = lax.optimization_barrier((first_rhs, factor[:block]))
    lower_first = lax.all_gather(first_rows, "pcol", axis=1, tiled=True)
    second_rows, _ = lax.optimization_barrier((factor[block:], lower_first))
    lower_second = lax.all_gather(second_rows, "pcol", axis=1, tiled=True)

    acc = jnp.zeros((rhs_width, block), jnp.float32)
    own = jnp.zeros((rhs_width, block), jnp.float32)
    for k in range(steps):
        if k == 0:
            solved = contract(first_rhs, inverses[:block])
        else:
            solved = contract(top_rhs - acc, inverses[k * block : (k + 1) * block])
        own = jnp.where(row_at == k, solved, own)
        if k == steps - 3:
            own_first = own
        if k == steps - 2:
            own_early = own
        if k == steps - 1:
            break
        if k == 0:
            arrived = solved
        else:
            arrived = jnp.zeros_like(solved)
            for i in range(k + 1, steps):
                pairs = [(at(k, c), at(i, c)) for c in range(n_col)]
                arrived = arrived + lax.ppermute(solved, AXES, pairs)
        acc = acc + contract(arrived, lower_first[:, k * block : (k + 1) * block])

    fan_z = min(steps, n_row // steps)
    stride_x = steps * fan_z
    spread = []
    for piece, sources in ((own_first, range(steps - 2)), (own_early, (steps - 2,)), (own, (steps - 1,))):
        for stride, fan in ((stride_x, n_row // stride_x), (steps, fan_z)):
            holders = [p for p in range(n_row) if p % (stride * fan) in sources]
            received = piece
            for hop in range(1, fan):
                pairs = [(p, p + hop * stride) for p in holders]
                arrived = lax.ppermute(piece, "prow", pairs)
                received = jnp.where((row_at % (stride * fan)) // stride == hop, arrived, received)
            piece = jnp.where(row_at % stride < steps, received, piece)
        spread.append(piece)
    piece = jnp.where(row_at % steps == steps - 1, spread[2], jnp.where(row_at % steps == steps - 2, spread[1], spread[0]))
    b0 = row_at % 2
    b1 = (row_at // 2) % 2
    other = lax.ppermute(piece, "prow", [(p, p ^ 2) for p in range(n_row)])
    pair = jnp.where(b1 == 0, jnp.concatenate([piece, other], axis=1), jnp.concatenate([other, piece], axis=1))
    theirs = lax.ppermute(pair, "prow", [(p, p ^ 1) for p in range(n_row)])
    mine, yours = (pair[:, :block], pair[:, block:]), (theirs[:, :block], theirs[:, block:])
    mine_first = jnp.concatenate([mine[0], yours[0], mine[1], yours[1]], axis=1)
    theirs_first = jnp.concatenate([yours[0], mine[0], yours[1], mine[1]], axis=1)
    panel = jnp.where(b0 == 0, mine_first, theirs_first)

    second = right_side[:, block:] - contract(panel, lower_second)
    first = right_side[:, :block] - contract(panel, lower_first)
    head_block = jnp.where(row_at < steps, own, first)
    return jnp.concatenate([head_block, second], axis=1)


def solution(mesh):
    return jax.shard_map(
        per_device,
        mesh=mesh,
        in_specs=(P("pcol", "prow"), P("prow", "pcol"), P()),
        out_specs=P("pcol", "prow"),
        check_vma=False,
    )
```
